128 devices in a mesh: dp: 8 (over z, core), expert: 16 (over x, y).
Axes of the slice: x: 4, y: 4, z: 4, core: 2. Of those that a mesh axis runs over, the one named last changes fastest.
Arguments:
- inputs: bfloat16 [16384, 3584], P(('dp', 'expert')), may hold values from -6 to 6
- out_grad: bfloat16 [16384, 3584], P(('dp', 'expert')), may hold values from -6 to 6
- expert_ids: int32 [16384, 2], P(('dp', 'expert')), may hold values from 0 to 15, all different within a row; in each aligned block of 128 rows (0 to 127, 128 to 255, ...) at most 24 rows name the same one
- gates: bfloat16 [16384, 2], P(('dp', 'expert')), may hold values from 0.099609375 to 1
- w_gate: bfloat16 [16, 1024, 3584], P('expert'), may hold values from -0.09375 to 0.09375
- w_up: bfloat16 [16, 1024, 3584], P('expert'), may hold values from -0.09375 to 0.09375
- w_down: bfloat16 [16, 1024, 3584], P('expert'), may hold values from -0.1875 to 0.1875
Outputs:
- input_grad: bfloat16 [16384, 3584], P(('dp', 'expert'))
- gate_grad: bfloat16 [16384, 2], P(('dp', 'expert'))
- grad_gate: bfloat16 [16, 1024, 3584], P('expert', 'dp')
- grad_up: bfloat16 [16, 1024, 3584], P('expert', 'dp')
- grad_down: bfloat16 [16, 1024, 3584], P('expert', 'dp')
The draws below stay inside these ranges and needn't reach their ends.
Inputs may be any that keep to these rules, and one draw needn't show every extreme that they name: `expert_ids`: within the 128 rows of one device, no expert is named by more than 24 pairs, and in every draw some device names some expert exactly 24 times; a token's 2 experts differ.
All inputs are finite; a program needn't handle non-finite values.
Results may differ from the reference program's by a relative error of at most 0.013.
Values may be sent and summed in bfloat16 or wider, within the bound.
No kernel may reach another device: no remote copies, remote signals or barrier semaphores. Data moves between devices by JAX's collectives and lax.ppermute only.
A program may use at most 192 MiB of HBM per device.

```python
import math
import jax
import jax.numpy as jnp
import numpy as np
from jax import lax

D = 3584
FF = 1024
TOP = 2
TOK_DEV = 128
CAP = 24
EXPERTS = 16
TOKENS = 16384
N_DP = 8
N_EXPERT = 16


def block_scale(stream_key, dims, cuts, low, top_value):
    def one(dim, parts):
        heights = jax.random.uniform(jax.random.fold_in(jax.random.fold_in(stream_key, 6), dim), (parts,), jnp.float32, low / len(cuts), top_value / len(cuts))
        return jnp.repeat(jnp.exp(heights), dims[dim] // parts).reshape((-1,) + (1,) * (len(dims) - dim - 1))

    loudness = one(*cuts[0])
    for cut in cuts[1:]:
        loudness = loudness * one(*cut)
    return loudness


def shared_out(own_key, own, number, rows, number_of, top, reach, skew):
    sequence = jax.random.permutation(own_key, number_of)
    crowded, usual = load_shares(number_of, rows * top, reach, skew, True), load_shares(number_of, rows * top, reach, skew, False)
    places = jnp.arange(number_of)

    def named(lengths, offset_by):
        used = int((lengths > 0).sum())
        fixed = max(1, used // 4)
        shifted = fixed + (places - fixed + offset_by * (used - fixed)) % max(1, number_of - fixed)
        return jnp.zeros((number_of,), jnp.int32).at[sequence[jnp.where(places < fixed, places, shifted)]].set(jnp.asarray(lengths, jnp.int32))

    lengths = jnp.where(number % 4 == 0, named(crowded, number // 4), named(usual, number - number // 4 - 1))
    mixed = jax.random.permutation(jax.random.fold_in(own, 3), number_of)
    giver, taker = mixed[0:number_of // 2 * 2:2], mixed[1:number_of // 2 * 2:2]
    slack = jnp.minimum(lengths[giver] - 1, reach - lengths[taker]) // 2
    slack = jnp.where((giver == sequence[0]) | (taker == sequence[0]) | (lengths[taker] == 0), 0, jnp.maximum(slack, 0))
    shifted = jax.random.randint(jax.random.fold_in(own, 4), (number_of // 2,), 0, 1 << 20) % (slack + 1)
    lengths = lengths.at[giver].add(-shifted).at[taker].add(shifted)
    labels = jnp.searchsorted(jnp.cumsum(lengths), jnp.arange(rows * top), side="right").astype(jnp.int32)
    table = labels.reshape(top, rows).T
    table = table[jax.random.permutation(jax.random.fold_in(own, 1), rows)]
    offset_by = jax.random.randint(jax.random.fold_in(own, 2), (rows, 1), 0, top)
    return jnp.take_along_axis(table, (jnp.arange(top)[None, :] + offset_by) % top, axis=1)


def load_shares(count, total, bound, lean, full):
    portions = [(1 << 20) // math.isqrt(standing ** lean) + 1 for standing in range(1, count + 1)]
    largest = bound if full else min(bound, max(-(-total // count), total * portions[0] // sum(portions)))
    least = 1 if total - largest >= count - 1 else 0
    holding, rest = [largest] + [least] * (count - 1), total - largest - least * (count - 1)
    while rest > 0:
        candidates = [i for i in range(1, count) if holding[i] < largest] or [i for i in range(1, count) if holding[i] < bound]
        pool, left = sum([portions[i] for i in candidates]), rest
        for i in candidates:
            addition = min(bound - holding[i], max(1, left * portions[i] // pool), rest)
            holding[i] = holding[i] + addition
            rest = rest - addition
    return np.array(holding)


def normal_values(key, extent, spread, reach, pieces=(), kind=jnp.bfloat16):
    values = spread * jax.random.normal(key, extent, jnp.float32)
    if pieces:
        values = values * block_scale(key, extent, pieces, -0.22, 0.18)
    return jnp.clip(values, -reach, reach).astype(kind)


def setup_inputs(seed: int = 0) -> dict:
    keys = jax.random.split(jax.random.key(seed), 8)
    inputs = normal_values(keys[0], (TOKENS, D), 1.0, 6.0, ((0, 128),))
    out_grad = normal_values(keys[1], (TOKENS, D), 1.0, 6.0, ((0, 128),))
    expert_ids_keys = jax.random.split(jax.random.fold_in(keys[2], 1), TOKENS // TOK_DEV)
    expert_ids_turns = jax.random.permutation(jax.random.fold_in(keys[2], 3), TOKENS // TOK_DEV)
    expert_ids = jax.vmap(lambda own, number: shared_out(jax.random.fold_in(keys[2], 2), own, number, TOK_DEV, EXPERTS, TOP, CAP, 2))(expert_ids_keys, expert_ids_turns).reshape((TOKENS, TOP))
    gates = jnp.clip(0.099609375 + 0.9003906 * jax.random.uniform(keys[3], (TOKENS, TOP), jnp.float32) ** block_scale(keys[3], (TOKENS, TOP), ((0, 128),), -0.2, 0.2), 0.099609375, 1.0).astype(jnp.bfloat16)
    w_gate = normal_values(keys[4], (EXPERTS, FF, D), D ** -0.5, 0.09375, ((0, 16),))
    w_up = normal_values(keys[5], (EXPERTS, FF, D), D ** -0.5, 0.09375, ((0, 16),))
    w_down = normal_values(keys[6], (EXPERTS, FF, D), FF ** -0.5, 0.1875, ((0, 16),))
    return {"inputs": inputs, "out_grad": out_grad, "expert_ids": expert_ids, "gates": gates, "w_gate": w_gate, "w_up": w_up, "w_down": w_down}


def build_tables(expert_ids, expert_count, capacity):
    token_count, top_count = expert_ids.shape
    flat_ids = expert_ids.reshape(-1)
    columns = jnp.arange(expert_count, dtype=jnp.int32)
    onehot = (flat_ids[:, None] == columns[None, :]).astype(jnp.int32)
    earlier = jnp.cumsum(onehot, axis=0) - onehot
    position = jnp.sum(earlier * onehot, axis=1).astype(jnp.int32)
    slot_index = flat_ids * capacity + position
    slot_range = jnp.arange(expert_count * capacity, dtype=jnp.int32)
    pair_table = (slot_index[:, None] == slot_range[None, :]).astype(jnp.bfloat16)
    token_table = jnp.sum(pair_table.reshape(token_count, top_count, -1).astype(jnp.float32), axis=1).astype(jnp.bfloat16)
    return pair_table, token_table


def contract_rows(left, right):
    return lax.dot_general(left, right, (((0,), (0,)), ((), ())), preferred_element_type=jnp.float32)


def times_weight(rows, weight):
    return lax.dot_general(rows, weight, (((1,), (1,)), ((), ())), preferred_element_type=jnp.float32)


def expert_pass(row_inputs, row_out_grads, row_gates, gate_matrix, up_matrix, down_matrix):
    gate_col = row_gates.astype(jnp.float32)[:, None]
    hidden_gate = times_weight(row_inputs, gate_matrix)
    hidden_up = times_weight(row_inputs, up_matrix)
    sigma = jax.nn.sigmoid(hidden_gate)
    activation = (hidden_gate * sigma * hidden_up).astype(jnp.bfloat16)
    scaled = (gate_col * row_out_grads.astype(jnp.float32)).astype(jnp.bfloat16)
    raw_grad = times_weight(row_out_grads, down_matrix)
    act_grad = gate_col * raw_grad
    gate_hidden = (act_grad * hidden_up * sigma * (1.0 + hidden_gate * (1.0 - sigma))).astype(jnp.bfloat16)
    up_hidden = (act_grad * hidden_gate * sigma).astype(jnp.bfloat16)
    row_back = (jnp.dot(gate_hidden, gate_matrix, preferred_element_type=jnp.float32)
                + jnp.dot(up_hidden, up_matrix, preferred_element_type=jnp.float32)).astype(jnp.bfloat16)
    expert_out = jnp.dot(activation, down_matrix, preferred_element_type=jnp.float32)
    pair_value = jnp.sum(row_out_grads.astype(jnp.float32) * expert_out, axis=1).astype(jnp.bfloat16)
    partials = jnp.stack([contract_rows(gate_hidden, row_inputs).astype(jnp.bfloat16),
                          contract_rows(up_hidden, row_inputs).astype(jnp.bfloat16),
                          contract_rows(activation, scaled).astype(jnp.bfloat16)])
    return row_back, pair_value, partials


def reference(inputs, out_grad, expert_ids, gates, w_gate, w_up, w_down):
    groups = N_DP
    owners = N_EXPERT
    devices_all = groups * owners
    ids_dev = expert_ids.reshape(devices_all, TOK_DEV, TOP)
    pair_tables, token_tables = jax.vmap(lambda block: build_tables(block, owners, CAP))(ids_dev)
    inputs_dev = inputs.reshape(devices_all, TOK_DEV, D)
    grads_dev = out_grad.reshape(devices_all, TOK_DEV, D)
    gates_dev = gates.reshape(devices_all, TOK_DEV * TOP)
    sent_inputs = jax.vmap(lambda table, rows: contract_rows(table, rows).astype(jnp.bfloat16))(token_tables, inputs_dev)
    sent_grads = jax.vmap(lambda table, rows: contract_rows(table, rows).astype(jnp.bfloat16))(token_tables, grads_dev)
    sent_gates = jax.vmap(lambda table, values: jnp.dot(values, table, preferred_element_type=jnp.float32).astype(jnp.bfloat16))(pair_tables, gates_dev)

    def to_owner(sent, tail):
        shaped = sent.reshape((groups, owners, owners, CAP) + tail)
        order = (2, 0, 1, 3) + tuple(range(4, 4 + len(tail)))
        return jnp.transpose(shaped, order).reshape((owners, groups, owners * CAP) + tail)

    owner_inputs = to_owner(sent_inputs, (D,))
    owner_grads = to_owner(sent_grads, (D,))
    owner_gates = to_owner(sent_gates, ())

    def one_expert(packed):
        x_groups, y_groups, g_groups, gate_matrix, up_matrix, down_matrix = packed

        def one_group(total, group):
            row_inputs, row_out_grads, row_gates = group
            row_back, pair_value, partials = expert_pass(row_inputs, row_out_grads, row_gates, gate_matrix, up_matrix, down_matrix)
            return total + partials.astype(jnp.float32), (row_back, pair_value)

        start = jnp.zeros((3, FF, D), jnp.float32)
        total, outputs = lax.scan(one_group, start, (x_groups, y_groups, g_groups))
        return total.astype(jnp.bfloat16), outputs[0], outputs[1]

    grads_all, backs, values = lax.map(one_expert, (owner_inputs, owner_grads, owner_gates, w_gate, w_up, w_down))
    backs = jnp.transpose(backs.reshape(owners, groups, owners, CAP, D), (1, 2, 0, 3, 4)).reshape(devices_all, owners * CAP, D)
    values = jnp.transpose(values.reshape(owners, groups, owners, CAP), (1, 2, 0, 3)).reshape(devices_all, owners * CAP)
    input_grad = jax.vmap(lambda table, rows: jnp.dot(table, rows, preferred_element_type=jnp.float32).astype(jnp.bfloat16))(token_tables, backs)
    gate_grad = jax.vmap(lambda table, vals: jnp.dot(table, vals, preferred_element_type=jnp.float32).astype(jnp.bfloat16))(pair_tables, values)
    return (input_grad.reshape(TOKENS, D), gate_grad.reshape(TOKENS, TOP),
            grads_all[:, 0], grads_all[:, 1], grads_all[:, 2])
```

```python
import jax
import jax.numpy as jnp
from jax import lax
from jax.sharding import PartitionSpec as P


def build_tables(expert_ids, expert_count, capacity):
    token_count, top_count = expert_ids.shape
    flat_ids = expert_ids.reshape(-1)
    columns = jnp.arange(expert_count, dtype=jnp.int32)
    onehot = (flat_ids[:, None] == columns[None, :]).astype(jnp.int32)
    earlier = jnp.cumsum(onehot, axis=0) - onehot
    position = jnp.sum(earlier * onehot, axis=1)
    slot_index = flat_ids * capacity + position
    slot_range = jnp.arange(expert_count * capacity, dtype=jnp.int32)
    pair_table = (slot_index[:, None] == slot_range[None, :]).astype(jnp.bfloat16)
    token_table = jnp.sum(
        pair_table.reshape(token_count, top_count, -1).astype(jnp.float32), axis=1
    ).astype(jnp.bfloat16)
    return (pair_table, token_table)


def contract_rows(left, right):
    return lax.dot_general(
        left, right, (((0,), (0,)), ((), ())), preferred_element_type=jnp.float32
    )


def times_weight(rows, weight):
    return lax.dot_general(
        rows, weight, (((1,), (1,)), ((), ())), preferred_element_type=jnp.float32
    )


LANES = 128


def shards(inputs, out_grad, expert_ids, gates, w_gate, w_up, w_down):
    token_count, width = inputs.shape
    top_count = expert_ids.shape[1]
    expert_count = lax.axis_size("expert")
    capacity = 3 * token_count * top_count // (2 * expert_count)
    slots = expert_count * capacity
    pair_table, token_table = build_tables(expert_ids, expert_count, capacity)

    both = jnp.concatenate([inputs, out_grad], axis=1)
    sent_rows = contract_rows(token_table, both).astype(jnp.bfloat16)
    sent_gates = jnp.dot(
        gates.reshape(-1), pair_table, preferred_element_type=jnp.float32
    ).astype(jnp.bfloat16)
    gate_block = jnp.zeros((slots, LANES), jnp.bfloat16).at[:, 0].set(sent_gates)
    packed = jnp.concatenate([sent_rows, gate_block], axis=1)
    recv = lax.all_to_all(
        packed.reshape(expert_count, capacity, -1),
        "expert",
        split_axis=0,
        concat_axis=0,
        tiled=True,
    ).reshape(slots, -1)
    row_inputs = recv[:, :width]
    row_out_grads = recv[:, width : 2 * width]
    gate_col = recv[:, 2 * width : 2 * width + 1].astype(jnp.float32)

    gate_matrix = w_gate[0]
    up_matrix = w_up[0]
    down_matrix = w_down[0]
    hidden_gate = times_weight(row_inputs, gate_matrix)
    hidden_up = times_weight(row_inputs, up_matrix)
    raw_grad = times_weight(row_out_grads, down_matrix)
    sigma = jax.nn.sigmoid(hidden_gate)
    activation = (hidden_gate * sigma * hidden_up).astype(jnp.bfloat16)
    scaled = (gate_col * row_out_grads.astype(jnp.float32)).astype(jnp.bfloat16)
    act_grad = gate_col * raw_grad
    gate_hidden = (act_grad * hidden_up * sigma * (1.0 + hidden_gate * (1.0 - sigma))).astype(
        jnp.bfloat16
    )
    up_hidden = (act_grad * hidden_gate * sigma).astype(jnp.bfloat16)

    def scatter(part):
        return lax.psum_scatter(
            part.astype(jnp.bfloat16), "dp", scatter_dimension=0, tiled=True
        )

    grad_gate = scatter(contract_rows(gate_hidden, row_inputs))
    grad_up = scatter(contract_rows(up_hidden, row_inputs))
    grad_down = scatter(contract_rows(activation, scaled))

    row_back = (
        jnp.dot(gate_hidden, gate_matrix, preferred_element_type=jnp.float32)
        + jnp.dot(up_hidden, up_matrix, preferred_element_type=jnp.float32)
    ).astype(jnp.bfloat16)
    pair_value = jnp.sum(activation.astype(jnp.float32) * raw_grad, axis=1).astype(
        jnp.bfloat16
    )
    value_block = jnp.zeros((slots, LANES), jnp.bfloat16).at[:, 0].set(pair_value)
    back = lax.all_to_all(
        jnp.concatenate([row_back, value_block], axis=1).reshape(
            expert_count, capacity, -1
        ),
        "expert",
        split_axis=0,
        concat_axis=0,
        tiled=True,
    ).reshape(slots, -1)
    back_rows = back[:, :width]
    back_values = back[:, width].astype(jnp.float32)
    input_grad = jnp.dot(
        token_table, back_rows, preferred_element_type=jnp.float32
    ).astype(jnp.bfloat16)
    gate_grad = (
        jnp.dot(pair_table.astype(jnp.float32), back_values, preferred_element_type=jnp.float32)
        .astype(jnp.bfloat16)
        .reshape(token_count, top_count)
    )
    return (input_grad, gate_grad, grad_gate[None], grad_up[None], grad_down[None])


def solution(mesh):
    in_specs = (
        P(("dp", "expert"), None),
        P(("dp", "expert"), None),
        P(("dp", "expert"), None),
        P(("dp", "expert"), None),
        P("expert", None, None),
        P("expert", None, None),
        P("expert", None, None),
    )
    out_specs = (
        P(("dp", "expert"), None),
        P(("dp", "expert"), None),
        P("expert", "dp", None),
        P("expert", "dp", None),
        P("expert", "dp", None),
    )
    return jax.shard_map(shards, mesh=mesh, in_specs=in_specs, out_specs=out_specs, check_vma=False)
```

```python
import jax
import jax.numpy as jnp
from jax import lax
from jax.sharding import PartitionSpec as P


def build_tables(expert_ids, expert_count, capacity):
    token_count, top_count = expert_ids.shape
    flat_ids = expert_ids.reshape(-1)
    columns = jnp.arange(expert_count, dtype=jnp.int32)
    onehot = (flat_ids[:, None] == columns[None, :]).astype(jnp.int32)
    earlier = jnp.cumsum(onehot, axis=0) - onehot
    position = jnp.sum(earlier * onehot, axis=1)
    slot_index = flat_ids * capacity + position
    slot_range = jnp.arange(expert_count * capacity, dtype=jnp.int32)
    pair_table = (slot_index[:, None] == slot_range[None, :]).astype(jnp.bfloat16)
    token_table = jnp.sum(
        pair_table.reshape(token_count, top_count, -1).astype(jnp.float32), axis=1
    ).astype(jnp.bfloat16)
    return (pair_table, token_table)


def contract_rows(left, right):
    return lax.dot_general(
        left, right, (((0,), (0,)), ((), ())), preferred_element_type=jnp.float32
    )


def times_weight(rows, weight):
    return lax.dot_general(
        rows, weight, (((1,), (1,)), ((), ())), preferred_element_type=jnp.float32
    )


LANES = 128


def shards(inputs, out_grad, expert_ids, gates, w_gate, w_up, w_down):
    token_count, width = inputs.shape
    top_count = expert_ids.shape[1]
    expert_count = lax.axis_size("expert")
    capacity = 3 * token_count * top_count // (2 * expert_count)
    slots = expert_count * capacity
    pair_table, token_table = build_tables(expert_ids, expert_count, capacity)

    both = jnp.concatenate([inputs, out_grad], axis=1)
    sent_rows = contract_rows(token_table, both).astype(jnp.bfloat16)
    sent_gates = jnp.dot(
        gates.reshape(-1), pair_table, preferred_element_type=jnp.float32
    ).astype(jnp.bfloat16)
    gate_block = jnp.zeros((slots, LANES), jnp.bfloat16).at[:, 0].set(sent_gates)
    packed = jnp.concatenate([sent_rows, gate_block], axis=1)
    recv = lax.all_to_all(
        packed.reshape(expert_count, capacity, -1),
        "expert",
        split_axis=0,
        concat_axis=0,
        tiled=True,
    ).reshape(slots, -1)
    row_inputs = recv[:, :width]
    row_out_grads = recv[:, width : 2 * width]
    gate_col = recv[:, 2 * width : 2 * width + 1].astype(jnp.float32)

    gate_matrix = w_gate[0]
    up_matrix = w_up[0]
    down_matrix = w_down[0]
    hidden_gate = times_weight(row_inputs, gate_matrix)
    hidden_up = times_weight(row_inputs, up_matrix)
    raw_grad = times_weight(row_out_grads, down_matrix)
    sigma = jax.nn.sigmoid(hidden_gate)
    activation = (hidden_gate * sigma * hidden_up).astype(jnp.bfloat16)
    scaled = (gate_col * row_out_grads.astype(jnp.float32)).astype(jnp.bfloat16)
    act_grad = gate_col * raw_grad
    gate_hidden = (act_grad * hidden_up * sigma * (1.0 + hidden_gate * (1.0 - sigma))).astype(
        jnp.bfloat16
    )
    up_hidden = (act_grad * hidden_gate * sigma).astype(jnp.bfloat16)

    n_z = lax.axis_size("z")
    n_core = lax.axis_size("core")

    def core_major(hidden):
        rows = hidden.shape[0]
        return (
            hidden.reshape(rows, n_z, n_core, -1)
            .transpose(0, 2, 1, 3)
            .reshape(rows, -1)
        )

    def scatter(part):
        part = part.astype(jnp.bfloat16).reshape(n_core, n_z, -1, width)
        part = lax.psum_scatter(part, "core", scatter_dimension=0, tiled=True)
        part = lax.psum_scatter(part, "z", scatter_dimension=1, tiled=True)
        return part.reshape(-1, width)

    grad_gate = scatter(contract_rows(core_major(gate_hidden), row_inputs))
    grad_up = scatter(contract_rows(core_major(up_hidden), row_inputs))
    grad_down = scatter(contract_rows(core_major(activation), scaled))

    row_back = (
        jnp.dot(gate_hidden, gate_matrix, preferred_element_type=jnp.float32)
        + jnp.dot(up_hidden, up_matrix, preferred_element_type=jnp.float32)
    ).astype(jnp.bfloat16)
    pair_value = jnp.sum(activation.astype(jnp.float32) * raw_grad, axis=1).astype(
        jnp.bfloat16
    )
    value_block = jnp.zeros((slots, LANES), jnp.bfloat16).at[:, 0].set(pair_value)
    back = lax.all_to_all(
        jnp.concatenate([row_back, value_block], axis=1).reshape(
            expert_count, capacity, -1
        ),
        "expert",
        split_axis=0,
        concat_axis=0,
        tiled=True,
    ).reshape(slots, -1)
    back_rows = back[:, :width]
    back_values = back[:, width].astype(jnp.float32)
    input_grad = jnp.dot(
        token_table, back_rows, preferred_element_type=jnp.float32
    ).astype(jnp.bfloat16)
    gate_grad = (
        jnp.dot(pair_table.astype(jnp.float32), back_values, preferred_element_type=jnp.float32)
        .astype(jnp.bfloat16)
        .reshape(token_count, top_count)
    )
    return (input_grad, gate_grad, grad_gate[None], grad_up[None], grad_down[None])


def solution(mesh):
    n_dp = mesh.shape["dp"]
    chip_mesh = jax.sharding.Mesh(
        mesh.devices.reshape(n_dp // 2, 2, mesh.shape["expert"]), ("z", "core", "expert")
    )
    tokens = P(("z", "core", "expert"), None)
    in_specs = (
        tokens,
        tokens,
        tokens,
        tokens,
        P("expert", None, None),
        P("expert", None, None),
        P("expert", None, None),
    )
    out_specs = (
        tokens,
        tokens,
        P("expert", ("z", "core"), None),
        P("expert", ("z", "core"), None),
        P("expert", ("z", "core"), None),
    )
    return jax.shard_map(shards, mesh=chip_mesh, in_specs=in_specs, out_specs=out_specs, check_vma=False)
```

```python
import jax
import jax.numpy as jnp
from jax import lax
from jax.sharding import PartitionSpec as P


def build_tables(expert_ids, expert_count, capacity):
    token_count, top_count = expert_ids.shape
    flat_ids = expert_ids.reshape(-1)
    columns = jnp.arange(expert_count, dtype=jnp.int32)
    onehot = (flat_ids[:, None] == columns[None, :]).astype(jnp.int32)
    earlier = jnp.cumsum(onehot, axis=0) - onehot
    position = jnp.sum(earlier * onehot, axis=1)
    slot_index = flat_ids * capacity + position
    slot_range = jnp.arange(expert_count * capacity, dtype=jnp.int32)
    pair_table = (slot_index[:, None] == slot_range[None, :]).astype(jnp.bfloat16)
    token_table = jnp.sum(
        pair_table.reshape(token_count, top_count, -1).astype(jnp.float32), axis=1
    ).astype(jnp.bfloat16)
    return (pair_table, token_table)


def contract_rows(left, right):
    return lax.dot_general(
        left, right, (((0,), (0,)), ((), ())), preferred_element_type=jnp.float32
    )


def times_weight(rows, weight):
    return lax.dot_general(
        rows, weight, (((1,), (1,)), ((), ())), preferred_element_type=jnp.float32
    )


LANES = 128


def shards(inputs, out_grad, expert_ids, gates, w_gate, w_up, w_down):
    token_count, width = inputs.shape
    top_count = expert_ids.shape[1]
    expert_count = lax.axis_size("expert")
    capacity = 3 * token_count * top_count // (2 * expert_count)
    slots = expert_count * capacity
    pair_table, token_table = build_tables(expert_ids, expert_count, capacity)

    both = jnp.concatenate([inputs, out_grad], axis=1)
    sent_rows = contract_rows(token_table, both).astype(jnp.bfloat16)
    sent_gates = jnp.dot(
        gates.reshape(-1), pair_table, preferred_element_type=jnp.float32
    ).astype(jnp.bfloat16)
    gate_block = jnp.zeros((slots, LANES), jnp.bfloat16).at[:, 0].set(sent_gates)
    packed = jnp.concatenate([sent_rows, gate_block], axis=1)
    recv = lax.all_to_all(
        packed.reshape(expert_count, capacity, -1),
        "expert",
        split_axis=0,
        concat_axis=0,
        tiled=True,
    ).reshape(slots, -1)
    row_inputs = recv[:, :width]
    row_out_grads = recv[:, width : 2 * width]
    gate_col = recv[:, 2 * width : 2 * width + 1].astype(jnp.float32)

    gate_matrix = w_gate[0]
    up_matrix = w_up[0]
    down_matrix = w_down[0]
    hidden_gate = times_weight(row_inputs, gate_matrix)
    hidden_up = times_weight(row_inputs, up_matrix)
    raw_grad = times_weight(row_out_grads, down_matrix)
    sigma = jax.nn.sigmoid(hidden_gate)
    activation = (hidden_gate * sigma * hidden_up).astype(jnp.bfloat16)
    scaled = (gate_col * row_out_grads.astype(jnp.float32)).astype(jnp.bfloat16)
    act_grad = gate_col * raw_grad
    gate_hidden = (act_grad * hidden_up * sigma * (1.0 + hidden_gate * (1.0 - sigma))).astype(
        jnp.bfloat16
    )
    up_hidden = (act_grad * hidden_gate * sigma).astype(jnp.bfloat16)

    lefts = jnp.stack([gate_hidden, up_hidden, activation])
    rights = jnp.stack([row_inputs, row_inputs, scaled])
    partials = lax.dot_general(
        lefts, rights, (((1,), (1,)), ((0,), (0,))), preferred_element_type=jnp.float32
    ).astype(jnp.bfloat16)
    joint = lax.psum_scatter(partials, "dp", scatter_dimension=1, tiled=True)
    grad_gate, grad_up, grad_down = joint[0], joint[1], joint[2]

    row_back = (
        jnp.dot(gate_hidden, gate_matrix, preferred_element_type=jnp.float32)
        + jnp.dot(up_hidden, up_matrix, preferred_element_type=jnp.float32)
    ).astype(jnp.bfloat16)
    pair_value = jnp.sum(activation.astype(jnp.float32) * raw_grad, axis=1).astype(
        jnp.bfloat16
    )
    value_block = jnp.zeros((slots, LANES), jnp.bfloat16).at[:, 0].set(pair_value)
    back = lax.all_to_all(
        jnp.concatenate([row_back, value_block], axis=1).reshape(
            expert_count, capacity, -1
        ),
        "expert",
        split_axis=0,
        concat_axis=0,
        tiled=True,
    ).reshape(slots, -1)
    back_rows = back[:, :width]
    back_values = back[:, width].astype(jnp.float32)
    input_grad = jnp.dot(
        token_table, back_rows, preferred_element_type=jnp.float32
    ).astype(jnp.bfloat16)
    gate_grad = (
        jnp.dot(pair_table.astype(jnp.float32), back_values, preferred_element_type=jnp.float32)
        .astype(jnp.bfloat16)
        .reshape(token_count, top_count)
    )
    return (input_grad, gate_grad, grad_gate[None], grad_up[None], grad_down[None])


def solution(mesh):
    in_specs = (
        P(("dp", "expert"), None),
        P(("dp", "expert"), None),
        P(("dp", "expert"), None),
        P(("dp", "expert"), None),
        P("expert", None, None),
        P("expert", None, None),
        P("expert", None, None),
    )
    out_specs = (
        P(("dp", "expert"), None),
        P(("dp", "expert"), None),
        P("expert", "dp", None),
        P("expert", "dp", None),
        P("expert", "dp", None),
    )
    return jax.shard_map(shards, mesh=mesh, in_specs=in_specs, out_specs=out_specs, check_vma=False)
```

```python
import jax
import jax.numpy as jnp
from jax import lax
from jax.sharding import PartitionSpec as P


def build_tables(expert_ids, expert_count, capacity):
    token_count, top_count = expert_ids.shape
    flat_ids = expert_ids.reshape(-1)
    columns = jnp.arange(expert_count, dtype=jnp.int32)
    onehot = (flat_ids[:, None] == columns[None, :]).astype(jnp.int32)
    earlier = jnp.cumsum(onehot, axis=0) - onehot
    position = jnp.sum(earlier * onehot, axis=1)
    slot_index = flat_ids * capacity + position
    slot_range = jnp.arange(expert_count * capacity, dtype=jnp.int32)
    pair_table = (slot_index[:, None] == slot_range[None, :]).astype(jnp.bfloat16)
    token_table = jnp.sum(
        pair_table.reshape(token_count, top_count, -1).astype(jnp.float32), axis=1
    ).astype(jnp.bfloat16)
    return (pair_table, token_table)


def contract_rows(left, right):
    return lax.dot_general(
        left, right, (((0,), (0,)), ((), ())), preferred_element_type=jnp.float32
    )


def times_weight(rows, weight):
    return lax.dot_general(
        rows, weight, (((1,), (1,)), ((), ())), preferred_element_type=jnp.float32
    )


LANES = 128


def shards(inputs, out_grad, expert_ids, gates, w_gate, w_up, w_down):
    token_count, width = inputs.shape
    top_count = expert_ids.shape[1]
    expert_count = lax.axis_size("expert")
    capacity = 3 * token_count * top_count // (2 * expert_count)
    slots = expert_count * capacity
    pair_table, token_table = build_tables(expert_ids, expert_count, capacity)

    def dispatch(rows):
        return lax.all_to_all(
            rows.reshape(expert_count, capacity, -1),
            "expert",
            split_axis=0,
            concat_axis=0,
            tiled=True,
        ).reshape(slots, -1)

    sent_gates = jnp.dot(
        gates.reshape(-1), pair_table, preferred_element_type=jnp.float32
    ).astype(jnp.bfloat16)
    gate_block = jnp.zeros((slots, LANES), jnp.bfloat16).at[:, 0].set(sent_gates)
    sent_inputs = contract_rows(token_table, inputs).astype(jnp.bfloat16)
    recv = dispatch(jnp.concatenate([sent_inputs, gate_block], axis=1))
    row_out_grads = dispatch(contract_rows(token_table, out_grad).astype(jnp.bfloat16))
    row_inputs = recv[:, :width]
    gate_col = recv[:, width : width + 1].astype(jnp.float32)

    gate_matrix = w_gate[0]
    up_matrix = w_up[0]
    down_matrix = w_down[0]
    hidden_gate = times_weight(row_inputs, gate_matrix)
    hidden_up = times_weight(row_inputs, up_matrix)
    raw_grad = times_weight(row_out_grads, down_matrix)
    sigma = jax.nn.sigmoid(hidden_gate)
    activation = (hidden_gate * sigma * hidden_up).astype(jnp.bfloat16)
    scaled = (gate_col * row_out_grads.astype(jnp.float32)).astype(jnp.bfloat16)
    act_grad = gate_col * raw_grad
    gate_hidden = (act_grad * hidden_up * sigma * (1.0 + hidden_gate * (1.0 - sigma))).astype(
        jnp.bfloat16
    )
    up_hidden = (act_grad * hidden_gate * sigma).astype(jnp.bfloat16)

    lefts = jnp.stack([gate_hidden, up_hidden, activation])
    rights = jnp.stack([row_inputs, row_inputs, scaled])
    partials = lax.dot_general(
        lefts, rights, (((1,), (1,)), ((0,), (0,))), preferred_element_type=jnp.float32
    ).astype(jnp.bfloat16)
    joint = lax.psum_scatter(partials, "dp", scatter_dimension=1, tiled=True)
    grad_gate, grad_up, grad_down = joint[0], joint[1], joint[2]

    row_back = (
        jnp.dot(gate_hidden, gate_matrix, preferred_element_type=jnp.float32)
        + jnp.dot(up_hidden, up_matrix, preferred_element_type=jnp.float32)
    ).astype(jnp.bfloat16)
    pair_value = jnp.sum(activation.astype(jnp.float32) * raw_grad, axis=1).astype(
        jnp.bfloat16
    )
    value_block = jnp.zeros((slots, LANES), jnp.bfloat16).at[:, 0].set(pair_value)
    back = lax.all_to_all(
        jnp.concatenate([row_back, value_block], axis=1).reshape(
            expert_count, capacity, -1
        ),
        "expert",
        split_axis=0,
        concat_axis=0,
        tiled=True,
    ).reshape(slots, -1)
    back_rows = back[:, :width]
    back_values = back[:, width].astype(jnp.float32)
    input_grad = jnp.dot(
        token_table, back_rows, preferred_element_type=jnp.float32
    ).astype(jnp.bfloat16)
    gate_grad = (
        jnp.dot(pair_table.astype(jnp.float32), back_values, preferred_element_type=jnp.float32)
        .astype(jnp.bfloat16)
        .reshape(token_count, top_count)
    )
    return (input_grad, gate_grad, grad_gate[None], grad_up[None], grad_down[None])


def solution(mesh):
    in_specs = (
        P(("dp", "expert"), None),
        P(("dp", "expert"), None),
        P(("dp", "expert"), None),
        P(("dp", "expert"), None),
        P("expert", None, None),
        P("expert", None, None),
        P("expert", None, None),
    )
    out_specs = (
        P(("dp", "expert"), None),
        P(("dp", "expert"), None),
        P("expert", "dp", None),
        P("expert", "dp", None),
        P("expert", "dp", None),
    )
    return jax.shard_map(shards, mesh=mesh, in_specs=in_specs, out_specs=out_specs, check_vma=False)
```

```python
import jax
import jax.numpy as jnp
from jax import lax
from jax.sharding import PartitionSpec as P


def build_tables(expert_ids, expert_count, capacity):
    token_count, top_count = expert_ids.shape
    flat_ids = expert_ids.reshape(-1)
    columns = jnp.arange(expert_count, dtype=jnp.int32)
    onehot = (flat_ids[:, None] == columns[None, :]).astype(jnp.int32)
    earlier = jnp.cumsum(onehot, axis=0) - onehot
    position = jnp.sum(earlier * onehot, axis=1)
    slot_index = flat_ids * capacity + position
    slot_range = jnp.arange(expert_count * capacity, dtype=jnp.int32)
    pair_table = (slot_index[:, None] == slot_range[None, :]).astype(jnp.bfloat16)
    token_table = jnp.sum(
        pair_table.reshape(token_count, top_count, -1).astype(jnp.float32), axis=1
    ).astype(jnp.bfloat16)
    return (pair_table, token_table)


def contract_rows(left, right):
    return lax.dot_general(
        left, right, (((0,), (0,)), ((), ())), preferred_element_type=jnp.float32
    )


def times_weight(rows, weight):
    return lax.dot_general(
        rows, weight, (((1,), (1,)), ((), ())), preferred_element_type=jnp.float32
    )


LANES = 128


def shards(inputs, out_grad, expert_ids, gates, w_gate, w_up, w_down):
    token_count, width = inputs.shape
    top_count = expert_ids.shape[1]
    expert_count = lax.axis_size("expert")
    capacity = 3 * token_count * top_count // (2 * expert_count)
    slots = expert_count * capacity
    pair_table, token_table = build_tables(expert_ids, expert_count, capacity)

    both = jnp.concatenate([inputs, out_grad], axis=1)
    sent_rows = contract_rows(token_table, both).astype(jnp.bfloat16)
    sent_gates = jnp.dot(
        gates.reshape(-1), pair_table, preferred_element_type=jnp.float32
    ).astype(jnp.bfloat16)
    gate_block = jnp.zeros((slots, LANES), jnp.bfloat16).at[:, 0].set(sent_gates)
    packed = jnp.concatenate([sent_rows, gate_block], axis=1)
    recv = lax.all_to_all(
        packed.reshape(expert_count, capacity, -1),
        "expert",
        split_axis=0,
        concat_axis=0,
        tiled=True,
    ).reshape(slots, -1)
    row_inputs = recv[:, :width]
    row_out_grads = recv[:, width : 2 * width]
    gate_col = recv[:, 2 * width : 2 * width + 1].astype(jnp.float32)

    n_dp = lax.axis_size("dp")
    hidden_count = w_gate.shape[1]
    halves = 2
    piece = hidden_count // (n_dp * halves)

    def half_of(weight, h):
        return weight[0].reshape(n_dp, halves, piece, width)[:, h].reshape(-1, width)

    scaled = (gate_col * row_out_grads.astype(jnp.float32)).astype(jnp.bfloat16)
    rights = jnp.stack([row_inputs, row_inputs, scaled])
    row_back = None
    pair_value = None
    joints = []
    for h in range(halves):
        gate_matrix = half_of(w_gate, h)
        up_matrix = half_of(w_up, h)
        down_matrix = half_of(w_down, h)
        hidden_gate = times_weight(row_inputs, gate_matrix)
        hidden_up = times_weight(row_inputs, up_matrix)
        raw_grad = times_weight(row_out_grads, down_matrix)
        sigma = jax.nn.sigmoid(hidden_gate)
        activation = (hidden_gate * sigma * hidden_up).astype(jnp.bfloat16)
        act_grad = gate_col * raw_grad
        gate_hidden = (
            act_grad * hidden_up * sigma * (1.0 + hidden_gate * (1.0 - sigma))
        ).astype(jnp.bfloat16)
        up_hidden = (act_grad * hidden_gate * sigma).astype(jnp.bfloat16)
        lefts = jnp.stack([gate_hidden, up_hidden, activation])
        partials = lax.dot_general(
            lefts, rights, (((1,), (1,)), ((0,), (0,))), preferred_element_type=jnp.float32
        ).astype(jnp.bfloat16)
        joints.append(lax.psum_scatter(partials, "dp", scatter_dimension=1, tiled=True))
        back_part = jnp.dot(
            gate_hidden, gate_matrix, preferred_element_type=jnp.float32
        ) + jnp.dot(up_hidden, up_matrix, preferred_element_type=jnp.float32)
        value_part = jnp.sum(activation.astype(jnp.float32) * raw_grad, axis=1)
        row_back = back_part if row_back is None else row_back + back_part
        pair_value = value_part if pair_value is None else pair_value + value_part
    row_back = row_back.astype(jnp.bfloat16)
    pair_value = pair_value.astype(jnp.bfloat16)
    joint = jnp.concatenate(joints, axis=1)
    grad_gate, grad_up, grad_down = joint[0], joint[1], joint[2]

    value_block = jnp.zeros((slots, LANES), jnp.bfloat16).at[:, 0].set(pair_value)
    back = lax.all_to_all(
        jnp.concatenate([row_back, value_block], axis=1).reshape(
            expert_count, capacity, -1
        ),
        "expert",
        split_axis=0,
        concat_axis=0,
        tiled=True,
    ).reshape(slots, -1)
    back_rows = back[:, :width]
    back_values = back[:, width].astype(jnp.float32)
    input_grad = jnp.dot(
        token_table, back_rows, preferred_element_type=jnp.float32
    ).astype(jnp.bfloat16)
    gate_grad = (
        jnp.dot(pair_table.astype(jnp.float32), back_values, preferred_element_type=jnp.float32)
        .astype(jnp.bfloat16)
        .reshape(token_count, top_count)
    )
    return (input_grad, gate_grad, grad_gate[None], grad_up[None], grad_down[None])


def solution(mesh):
    in_specs = (
        P(("dp", "expert"), None),
        P(("dp", "expert"), None),
        P(("dp", "expert"), None),
        P(("dp", "expert"), None),
        P("expert", None, None),
        P("expert", None, None),
        P("expert", None, None),
    )
    out_specs = (
        P(("dp", "expert"), None),
        P(("dp", "expert"), None),
        P("expert", "dp", None),
        P("expert", "dp", None),
        P("expert", "dp", None),
    )
    return jax.shard_map(shards, mesh=mesh, in_specs=in_specs, out_specs=out_specs, check_vma=False)
```

```python
import jax
import jax.numpy as jnp
from jax import lax
from jax.sharding import PartitionSpec as P


def build_tables(expert_ids, expert_count, capacity):
    token_count, top_count = expert_ids.shape
    columns = jnp.arange(expert_count, dtype=jnp.int32)
    onehots = [
        (expert_ids[:, k][:, None] == columns[None, :]).astype(jnp.bfloat16)
        for k in range(top_count)
    ]
    rows = jnp.arange(token_count, dtype=jnp.int32)
    before = (rows[None, :] < rows[:, None]).astype(jnp.bfloat16)
    earlier = jnp.dot(before, sum(onehots), preferred_element_type=jnp.float32)
    slot_range = jnp.arange(expert_count * capacity, dtype=jnp.int32)
    pair_tables = []
    for k in range(top_count):
        position = jnp.sum(earlier * onehots[k].astype(jnp.float32), axis=1)
        earlier = earlier + onehots[k].astype(jnp.float32)
        slot_index = expert_ids[:, k] * capacity + position.astype(jnp.int32)
        pair_tables.append(
            (slot_index[:, None] == slot_range[None, :]).astype(jnp.bfloat16)
        )
    token_table = sum(pair_tables)
    return (pair_tables, token_table)


def contract_rows(left, right):
    return lax.dot_general(
        left, right, (((0,), (0,)), ((), ())), preferred_element_type=jnp.float32
    )


def times_weight(rows, weight):
    return lax.dot_general(
        rows, weight, (((1,), (1,)), ((), ())), preferred_element_type=jnp.float32
    )


LANES = 128


def shards(inputs, out_grad, expert_ids, gates, w_gate, w_up, w_down):
    token_count, width = inputs.shape
    top_count = expert_ids.shape[1]
    expert_count = lax.axis_size("expert")
    capacity = 3 * token_count * top_count // (2 * expert_count)
    slots = expert_count * capacity
    pair_table, token_table = build_tables(expert_ids, expert_count, capacity)

    both = jnp.concatenate([inputs, out_grad], axis=1)
    sent_rows = contract_rows(token_table, both).astype(jnp.bfloat16)
    sent_gates = sum(
        jnp.dot(gates[:, k], pair_table[k], preferred_element_type=jnp.float32)
        for k in range(top_count)
    ).astype(jnp.bfloat16)
    gate_block = jnp.zeros((slots, LANES), jnp.bfloat16).at[:, 0].set(sent_gates)
    packed = jnp.concatenate([sent_rows, gate_block], axis=1)
    recv = lax.all_to_all(
        packed.reshape(expert_count, capacity, -1),
        "expert",
        split_axis=0,
        concat_axis=0,
        tiled=True,
    ).reshape(slots, -1)
    row_inputs = recv[:, :width]
    row_out_grads = recv[:, width : 2 * width]
    gate_col = recv[:, 2 * width : 2 * width + 1].astype(jnp.float32)

    gate_matrix = w_gate[0]
    up_matrix = w_up[0]
    down_matrix = w_down[0]
    hidden_gate = times_weight(row_inputs, gate_matrix)
    hidden_up = times_weight(row_inputs, up_matrix)
    raw_grad = times_weight(row_out_grads, down_matrix)
    sigma = jax.nn.sigmoid(hidden_gate)
    activation = (hidden_gate * sigma * hidden_up).astype(jnp.bfloat16)
    scaled = (gate_col * row_out_grads.astype(jnp.float32)).astype(jnp.bfloat16)
    act_grad = gate_col * raw_grad
    gate_hidden = (act_grad * hidden_up * sigma * (1.0 + hidden_gate * (1.0 - sigma))).astype(
        jnp.bfloat16
    )
    up_hidden = (act_grad * hidden_gate * sigma).astype(jnp.bfloat16)

    lefts = jnp.stack([gate_hidden, up_hidden, activation])
    rights = jnp.stack([row_inputs, row_inputs, scaled])
    partials = lax.dot_general(
        lefts, rights, (((1,), (1,)), ((0,), (0,))), preferred_element_type=jnp.float32
    ).astype(jnp.bfloat16)
    joint = lax.psum_scatter(partials, "dp", scatter_dimension=1, tiled=True)
    grad_gate, grad_up, grad_down = joint[0], joint[1], joint[2]

    row_back = (
        jnp.dot(gate_hidden, gate_matrix, preferred_element_type=jnp.float32)
        + jnp.dot(up_hidden, up_matrix, preferred_element_type=jnp.float32)
    ).astype(jnp.bfloat16)
    pair_value = jnp.sum(activation.astype(jnp.float32) * raw_grad, axis=1).astype(
        jnp.bfloat16
    )
    value_block = jnp.zeros((slots, LANES), jnp.bfloat16).at[:, 0].set(pair_value)
    back = lax.all_to_all(
        jnp.concatenate([row_back, value_block], axis=1).reshape(
            expert_count, capacity, -1
        ),
        "expert",
        split_axis=0,
        concat_axis=0,
        tiled=True,
    ).reshape(slots, -1)
    back_rows = back[:, :width]
    back_values = back[:, width].astype(jnp.float32)
    input_grad = jnp.dot(
        token_table, back_rows, preferred_element_type=jnp.float32
    ).astype(jnp.bfloat16)
    gate_grad = jnp.stack(
        [
            jnp.dot(table.astype(jnp.float32), back_values, preferred_element_type=jnp.float32)
            for table in pair_table
        ],
        axis=1,
    ).astype(jnp.bfloat16)
    return (input_grad, gate_grad, grad_gate[None], grad_up[None], grad_down[None])


def solution(mesh):
    in_specs = (
        P(("dp", "expert"), None),
        P(("dp", "expert"), None),
        P(("dp", "expert"), None),
        P(("dp", "expert"), None),
        P("expert", None, None),
        P("expert", None, None),
        P("expert", None, None),
    )
    out_specs = (
        P(("dp", "expert"), None),
        P(("dp", "expert"), None),
        P("expert", "dp", None),
        P("expert", "dp", None),
        P("expert", "dp", None),
    )
    return jax.shard_map(shards, mesh=mesh, in_specs=in_specs, out_specs=out_specs, check_vma=False)
```

```python
import jax
import jax.numpy as jnp
from jax import lax
from jax.sharding import PartitionSpec as P


def build_tables(expert_ids, expert_count, capacity):
    token_count, top_count = expert_ids.shape
    columns = jnp.arange(expert_count, dtype=jnp.int32)
    onehot = (expert_ids[:, :, None] == columns[None, None, :]).astype(jnp.bfloat16)
    onehots = [onehot[:, k] for k in range(top_count)]
    rows = jnp.arange(token_count, dtype=jnp.int32)
    before = (rows[None, :] < rows[:, None]).astype(jnp.bfloat16)
    earlier = jnp.dot(before, sum(onehots), preferred_element_type=jnp.float32)
    slot_range = jnp.arange(expert_count * capacity, dtype=jnp.int32)
    pair_tables = []
    for k in range(top_count):
        position = jnp.sum(earlier * onehots[k].astype(jnp.float32), axis=1)
        earlier = earlier + onehots[k].astype(jnp.float32)
        slot_index = expert_ids[:, k] * capacity + position.astype(jnp.int32)
        pair_tables.append(
            (slot_index[:, None] == slot_range[None, :]).astype(jnp.bfloat16)
        )
    token_table = sum(pair_tables)
    return (pair_tables, token_table)


def contract_rows(left, right):
    return lax.dot_general(
        left, right, (((0,), (0,)), ((), ())), preferred_element_type=jnp.float32
    )


def times_weight(rows, weight):
    return lax.dot_general(
        rows, weight, (((1,), (1,)), ((), ())), preferred_element_type=jnp.float32
    )


LANES = 128


def lane_block(values):
    lane = lax.broadcasted_iota(jnp.int32, (values.shape[0], LANES), 1)
    return jnp.where(lane == 0, values[:, None], jnp.zeros((), values.dtype))


def shards(inputs, out_grad, expert_ids, gates, w_gate, w_up, w_down):
    token_count, width = inputs.shape
    top_count = expert_ids.shape[1]
    expert_count = lax.axis_size("expert")
    capacity = 3 * token_count * top_count // (2 * expert_count)
    slots = expert_count * capacity
    pair_table, token_table = build_tables(expert_ids, expert_count, capacity)

    both = jnp.concatenate([inputs, out_grad], axis=1)
    per_choice = jnp.stack(
        [jnp.concatenate([both, lane_block(gates[:, k])], axis=1) for k in range(top_count)]
    )
    packed = lax.dot_general(
        jnp.stack(pair_table),
        per_choice,
        (((0, 1), (0, 1)), ((), ())),
        preferred_element_type=jnp.float32,
    ).astype(jnp.bfloat16)
    recv = lax.all_to_all(
        packed.reshape(expert_count, capacity, -1),
        "expert",
        split_axis=0,
        concat_axis=0,
        tiled=True,
    ).reshape(slots, -1)
    row_inputs = recv[:, :width]
    row_out_grads = recv[:, width : 2 * width]
    gate_col = recv[:, 2 * width : 2 * width + 1].astype(jnp.float32)

    gate_matrix = w_gate[0]
    up_matrix = w_up[0]
    down_matrix = w_down[0]
    hidden_gate = times_weight(row_inputs, gate_matrix)
    hidden_up = times_weight(row_inputs, up_matrix)
    raw_grad = times_weight(row_out_grads, down_matrix)
    sigma = jax.nn.sigmoid(hidden_gate)
    activation = (hidden_gate * sigma * hidden_up).astype(jnp.bfloat16)
    scaled = (gate_col * row_out_grads.astype(jnp.float32)).astype(jnp.bfloat16)
    act_grad = gate_col * raw_grad
    gate_hidden = (act_grad * hidden_up * sigma * (1.0 + hidden_gate * (1.0 - sigma))).astype(
        jnp.bfloat16
    )
    up_hidden = (act_grad * hidden_gate * sigma).astype(jnp.bfloat16)

    lefts = jnp.stack([gate_hidden, up_hidden, activation])
    rights = jnp.stack([row_inputs, row_inputs, scaled])
    partials = lax.dot_general(
        lefts, rights, (((1,), (1,)), ((0,), (0,))), preferred_element_type=jnp.float32
    ).astype(jnp.bfloat16)
    joint = lax.psum_scatter(partials, "dp", scatter_dimension=1, tiled=True)
    grad_gate, grad_up, grad_down = joint[0], joint[1], joint[2]

    row_back = (
        jnp.dot(gate_hidden, gate_matrix, preferred_element_type=jnp.float32)
        + jnp.dot(up_hidden, up_matrix, preferred_element_type=jnp.float32)
    ).astype(jnp.bfloat16)
    pair_value = jnp.sum(activation.astype(jnp.float32) * raw_grad, axis=1).astype(
        jnp.bfloat16
    )
    value_block = lane_block(pair_value)
    back = lax.all_to_all(
        jnp.concatenate([row_back, value_block], axis=1).reshape(
            expert_count, capacity, -1
        ),
        "expert",
        split_axis=0,
        concat_axis=0,
        tiled=True,
    ).reshape(slots, -1)
    back_rows = back[:, :width]
    back_values = back[:, width].astype(jnp.float32)
    input_grad = jnp.dot(
        token_table, back_rows, preferred_element_type=jnp.float32
    ).astype(jnp.bfloat16)
    gate_grad = jnp.stack(
        [
            jnp.dot(table.astype(jnp.float32), back_values, preferred_element_type=jnp.float32)
            for table in pair_table
        ],
        axis=1,
    ).astype(jnp.bfloat16)
    return (input_grad, gate_grad, grad_gate[None], grad_up[None], grad_down[None])


def solution(mesh):
    in_specs = (
        P(("dp", "expert"), None),
        P(("dp", "expert"), None),
        P(("dp", "expert"), None),
        P(("dp", "expert"), None),
        P("expert", None, None),
        P("expert", None, None),
        P("expert", None, None),
    )
    out_specs = (
        P(("dp", "expert"), None),
        P(("dp", "expert"), None),
        P("expert", "dp", None),
        P("expert", "dp", None),
        P("expert", "dp", None),
    )
    return jax.shard_map(shards, mesh=mesh, in_specs=in_specs, out_specs=out_specs, check_vma=False)
```

```python
import jax
import jax.numpy as jnp
from jax import lax
from jax.sharding import PartitionSpec as P


def build_tables(expert_ids, expert_count, capacity):
    token_count, top_count = expert_ids.shape
    columns = jnp.arange(expert_count, dtype=jnp.int32)
    onehot = (expert_ids[:, :, None] == columns[None, None, :]).astype(jnp.bfloat16)
    onehots = [onehot[:, k] for k in range(top_count)]
    rows = jnp.arange(token_count, dtype=jnp.int32)
    before = (rows[None, :] < rows[:, None]).astype(jnp.bfloat16)
    earlier = jnp.dot(before, sum(onehots), preferred_element_type=jnp.float32)
    slot_range = jnp.arange(expert_count * capacity, dtype=jnp.int32)
    pair_tables = []
    for k in range(top_count):
        position = jnp.sum(earlier * onehots[k].astype(jnp.float32), axis=1)
        earlier = earlier + onehots[k].astype(jnp.float32)
        slot_index = expert_ids[:, k] * capacity + position.astype(jnp.int32)
        pair_tables.append(
            (slot_index[:, None] == slot_range[None, :]).astype(jnp.bfloat16)
        )
    token_table = sum(pair_tables)
    return (pair_tables, token_table)


def contract_rows(left, right):
    return lax.dot_general(
        left, right, (((0,), (0,)), ((), ())), preferred_element_type=jnp.float32
    )


def times_weight(rows, weight):
    return lax.dot_general(
        rows, weight, (((1,), (1,)), ((), ())), preferred_element_type=jnp.float32
    )


LANES = 128


def lane_block(values):
    lane = lax.broadcasted_iota(jnp.int32, (values.shape[0], LANES), 1)
    return jnp.where(lane == 0, values[:, None], jnp.zeros((), values.dtype))


def shards(inputs, out_grad, expert_ids, gates, w_gate, w_up, w_down):
    token_count, width = inputs.shape
    top_count = expert_ids.shape[1]
    expert_count = lax.axis_size("expert")
    capacity = 3 * token_count * top_count // (2 * expert_count)
    slots = expert_count * capacity
    pair_table, token_table = build_tables(expert_ids, expert_count, capacity)

    lane = lax.broadcasted_iota(jnp.int32, (token_count, LANES), 1)
    choice_lanes = jnp.zeros((token_count, LANES), jnp.bfloat16)
    for k in range(top_count):
        choice_lanes = jnp.where(lane == k, gates[:, k][:, None], choice_lanes)
        choice_lanes = jnp.where(
            lane == top_count + k, expert_ids[:, k][:, None].astype(jnp.bfloat16), choice_lanes
        )
    packed = contract_rows(
        token_table, jnp.concatenate([inputs, out_grad, choice_lanes], axis=1)
    ).astype(jnp.bfloat16)
    recv = lax.all_to_all(
        packed.reshape(expert_count, capacity, -1),
        "expert",
        split_axis=0,
        concat_axis=0,
        tiled=True,
    ).reshape(slots, -1)
    row_inputs = recv[:, :width]
    row_out_grads = recv[:, width : 2 * width]
    own = lax.axis_index("expert").astype(jnp.float32)
    gate = recv[:, 2 * width + top_count - 1].astype(jnp.float32)
    for k in range(top_count - 1):
        named = recv[:, 2 * width + top_count + k].astype(jnp.float32)
        gate = jnp.where(named == own, recv[:, 2 * width + k].astype(jnp.float32), gate)
    gate_col = gate[:, None]

    gate_matrix = w_gate[0]
    up_matrix = w_up[0]
    down_matrix = w_down[0]
    hidden_gate = times_weight(row_inputs, gate_matrix)
    hidden_up = times_weight(row_inputs, up_matrix)
    raw_grad = times_weight(row_out_grads, down_matrix)
    sigma = jax.nn.sigmoid(hidden_gate)
    activation = (hidden_gate * sigma * hidden_up).astype(jnp.bfloat16)
    scaled = (gate_col * row_out_grads.astype(jnp.float32)).astype(jnp.bfloat16)
    act_grad = gate_col * raw_grad
    gate_hidden = (act_grad * hidden_up * sigma * (1.0 + hidden_gate * (1.0 - sigma))).astype(
        jnp.bfloat16
    )
    up_hidden = (act_grad * hidden_gate * sigma).astype(jnp.bfloat16)

    lefts = jnp.stack([gate_hidden, up_hidden, activation])
    rights = jnp.stack([row_inputs, row_inputs, scaled])
    partials = lax.dot_general(
        lefts, rights, (((1,), (1,)), ((0,), (0,))), preferred_element_type=jnp.float32
    ).astype(jnp.bfloat16)
    joint = lax.psum_scatter(partials, "dp", scatter_dimension=1, tiled=True)
    grad_gate, grad_up, grad_down = joint[0], joint[1], joint[2]

    row_back = (
        jnp.dot(gate_hidden, gate_matrix, preferred_element_type=jnp.float32)
        + jnp.dot(up_hidden, up_matrix, preferred_element_type=jnp.float32)
    ).astype(jnp.bfloat16)
    pair_value = jnp.sum(activation.astype(jnp.float32) * raw_grad, axis=1).astype(
        jnp.bfloat16
    )
    value_block = lane_block(pair_value)
    back = lax.all_to_all(
        jnp.concatenate([row_back, value_block], axis=1).reshape(
            expert_count, capacity, -1
        ),
        "expert",
        split_axis=0,
        concat_axis=0,
        tiled=True,
    ).reshape(slots, -1)
    back_rows = back[:, :width]
    back_values = back[:, width].astype(jnp.float32)
    input_grad = jnp.dot(
        token_table, back_rows, preferred_element_type=jnp.float32
    ).astype(jnp.bfloat16)
    gate_grad = jnp.stack(
        [
            jnp.dot(table.astype(jnp.float32), back_values, preferred_element_type=jnp.float32)
            for table in pair_table
        ],
        axis=1,
    ).astype(jnp.bfloat16)
    return (input_grad, gate_grad, grad_gate[None], grad_up[None], grad_down[None])


def solution(mesh):
    in_specs = (
        P(("dp", "expert"), None),
        P(("dp", "expert"), None),
        P(("dp", "expert"), None),
        P(("dp", "expert"), None),
        P("expert", None, None),
        P("expert", None, None),
        P("expert", None, None),
    )
    out_specs = (
        P(("dp", "expert"), None),
        P(("dp", "expert"), None),
        P("expert", "dp", None),
        P("expert", "dp", None),
        P("expert", "dp", None),
    )
    return jax.shard_map(shards, mesh=mesh, in_specs=in_specs, out_specs=out_specs, check_vma=False)
```
